32 devices in a mesh: rep: 2 (over x), seq: 16 (over z, y, core).
Axes of the slice: x: 2, y: 2, z: 4, core: 2. Of those that a mesh axis runs over, the one named last changes fastest.
Arguments:
- signal: bfloat16 [8192, 2048], P(('rep', 'seq')), parts along dimension 0, may hold values from -6 to 6
- gate: bfloat16 [8192, 2048], P(('rep', 'seq')), parts along dimension 0, may hold values from -6 to 6
- skip: float32 [2048], replicated, may hold values from -4 to 4
- taps: bfloat16 [1024, 128], P('seq'), may hold values from -2 to 2
Outputs:
- mixed: bfloat16 [8192, 2048], P(('rep', 'seq')), parts along dimension 0
The draws below stay inside these ranges and needn't reach their ends.
There are 2 independent parts, one for each index of `rep`. The reference program is written for one: setup_inputs(seed, part) draws one part's arguments, and reference() takes and returns one part's arrays. A program takes and returns all parts, laid end to end along the dimension named above; an argument that names none is the same for every part. Nothing has to cross between parts.
All inputs are finite; a program needn't handle non-finite values.
Results may differ from the reference program's by a relative error of at most 0.001.
Values may be sent and summed in bfloat16 or wider, within the bound.
No kernel may reach another device: no remote copies, remote signals or barrier semaphores. Data moves between devices by JAX's collectives and lax.ppermute only.
A program may use at most 128 MiB of HBM per device.

```python
import math
import jax
import jax.numpy as jnp
from jax import lax

CHAN = 2048
GROUP_WIDTH = 16
GROUPS = 128
FILTER_LEN = 1024
SEQ_LEN = 4096


def draw_taps(key, part):
    first_key = jax.random.fold_in(key, 11)
    second_key = jax.random.fold_in(key, 12)
    lagged = jnp.arange(FILTER_LEN, dtype=jnp.float32)[:, None]
    decay_len = jnp.exp(jax.random.uniform(first_key, (1, GROUPS), jnp.float32, math.log(20.0), math.log(4.0 * FILTER_LEN)))
    rough = jax.random.truncated_normal(second_key, -4.0, 4.0, (FILTER_LEN, GROUPS), jnp.float32)
    energy = 0.5 * decay_len * (1.0 - jnp.exp(-2.0 * FILTER_LEN / decay_len))
    values = rough * jnp.exp(-lagged / decay_len) / jnp.sqrt(energy)
    return values.astype(jnp.bfloat16)


def level_of(key, dims, shards, low, largest):
    level = 1.0
    for dim, blocks in shards:
        heights = jax.random.uniform(jax.random.fold_in(jax.random.fold_in(key, 6), dim), (blocks,), jnp.float32, low / len(shards), largest / len(shards))
        level = level * jnp.repeat(jnp.exp(heights), dims[dim] // blocks).reshape((-1,) + (1,) * (len(dims) - 1 - dim))
    return level


def noise(own_key, dims, deviation, reach, cuts=(), kind=jnp.bfloat16):
    result = deviation * jax.random.normal(own_key, dims, jnp.float32)
    if cuts:
        result = result * level_of(own_key, dims, cuts, -0.22, 0.18)
    return jnp.clip(result, -reach, reach).astype(kind)


def setup_inputs(seed: int = 0, part: int = 0) -> dict:
    key_list = jax.random.split(jax.random.key(seed), 5)
    part_splits = jax.random.split(jax.random.fold_in(key_list[4], part), 5)
    signal = noise(part_splits[0], (SEQ_LEN, CHAN), 1.0, 6.0, ((0, 16),))
    gate = noise(part_splits[1], (SEQ_LEN, CHAN), 1.0, 6.0, ((0, 16),))
    skip = noise(key_list[2], (CHAN,), 1.0, 4.0, (), jnp.float32)
    taps = draw_taps(jax.random.fold_in(key_list[4], 71), part)
    return dict(signal=signal, gate=gate, skip=skip, taps=taps)


def reference(signal, gate, skip, taps):
    total_len = signal.shape[0]
    filter_len = taps.shape[0]
    fft_len = 2 ** int(math.ceil(math.log2(total_len + filter_len)))
    per_channel = jnp.repeat(taps.astype(jnp.float32), GROUP_WIDTH, axis=1)
    block_width = min(128, CHAN)
    inputs = signal.astype(jnp.float32).T.reshape(CHAN // block_width, block_width, total_len)
    filters = per_channel.T.reshape(CHAN // block_width, block_width, filter_len)

    def convolve(paired):
        spectrum = jnp.fft.rfft(paired[0], fft_len) * jnp.fft.rfft(paired[1], fft_len)
        return jnp.fft.irfft(spectrum, fft_len)[:, :total_len]

    outputs = lax.map(convolve, (inputs, filters))
    convolved = outputs.reshape(CHAN, total_len).T.astype(jnp.float32)
    mixed = gate.astype(jnp.float32) * (convolved + skip[None, :] * signal.astype(jnp.float32))
    return mixed.astype(jnp.bfloat16)
```

```python
import functools

import jax
import jax.numpy as jnp
from jax import lax
from jax.experimental import pallas as pl
from jax.experimental.pallas import tpu as pltpu
from jax.sharding import PartitionSpec as P

TILE = 128
LANES = 128


def from_behind(shard, axis, by):
    count = lax.axis_size(axis)
    pairs = [(i, i + by) for i in range(count) if 0 <= i + by < count]
    return lax.ppermute(shard, axis, pairs)


def tap_rows(all_taps, history):
    filter_len, group_count = all_taps.shape
    flipped = all_taps.T[:, ::-1].astype(jnp.float32)
    front = jnp.zeros((group_count, TILE + history - filter_len + 1), jnp.float32)
    back = jnp.zeros((group_count, TILE - 1), jnp.float32)
    return jnp.concatenate([front, flipped, back], axis=1)


def conv_kernel(rows_ref, *refs, hops, group_width):
    blocks = refs[:hops + 1]
    gate_ref, skip_ref, out_ref = refs[hops + 1:]
    block_rows = blocks[0].shape[0]
    groups_here = rows_ref.shape[0]
    span = hops * block_rows + TILE
    sub_tiles = span // TILE
    out_tiles = block_rows // TILE
    x = jnp.concatenate([b[...] for b in blocks], axis=0)
    w = jnp.concatenate(
        [x[i * TILE: i * TILE + span] for i in range(out_tiles)], axis=1)
    lane_group = lax.broadcasted_iota(jnp.int32, w.shape, 1) % LANES // group_width
    upper = (lax.broadcasted_iota(jnp.int32, (TILE, TILE), 1)
             >= lax.broadcasted_iota(jnp.int32, (TILE, TILE), 0))
    acc = jnp.zeros((TILE, w.shape[1]), jnp.float32)
    for gg in range(groups_here):
        rolled = []
        for k in range(sub_tiles + 1):
            window = rows_ref[gg:gg + 1, k * TILE:(k + 1) * TILE]
            window = jnp.broadcast_to(window, (TILE, TILE))
            rolled.append(pltpu.roll(window, 0, 1, stride=1, stride_axis=0))
        toeplitz = jnp.concatenate(
            [jnp.where(upper, rolled[k + 1], rolled[k]) for k in range(sub_tiles)],
            axis=1).astype(jnp.bfloat16)
        masked = jnp.where(lane_group == gg, w, jnp.zeros_like(w))
        acc = acc + jnp.dot(toeplitz, masked, preferred_element_type=jnp.float32)
    conv = jnp.concatenate(
        [acc[:, i * LANES:(i + 1) * LANES] for i in range(out_tiles)], axis=0)
    cur = blocks[hops][...].astype(jnp.float32)
    mixed = gate_ref[...].astype(jnp.float32) * (conv + skip_ref[...] * cur)
    out_ref[...] = mixed.astype(out_ref.dtype)


def convolve(rows, blocks, gate, skip, group_width):
    hops = len(blocks) - 1
    block_rows, channels = gate.shape
    chunks = channels // LANES
    groups_per = LANES // group_width
    block_spec = pl.BlockSpec((block_rows, LANES), lambda c: (0, c))
    kernel = functools.partial(conv_kernel, hops=hops, group_width=group_width)
    return pl.pallas_call(
        kernel,
        grid=(chunks,),
        in_specs=[pl.BlockSpec((groups_per, rows.shape[1]), lambda c: (c, 0))]
        + [block_spec] * (hops + 1)
        + [block_spec, pl.BlockSpec((1, LANES), lambda c: (0, c))],
        out_specs=block_spec,
        out_shape=jax.ShapeDtypeStruct(gate.shape, gate.dtype),
        compiler_params=pltpu.CompilerParams(dimension_semantics=("arbitrary",)),
    )(rows, *blocks, gate, skip.reshape(1, channels))


def body(signal, gate, skip, taps):
    block_rows, channels = signal.shape
    group_count = taps.shape[1]
    group_width = channels // group_count
    all_taps = lax.all_gather(taps, "seq", axis=0, tiled=True)
    filter_len = all_taps.shape[0]
    hops = -(-(filter_len - 1) // block_rows)
    all_taps, signal = lax.optimization_barrier((all_taps, signal))
    received = [from_behind(signal, "seq", d) for d in range(hops, 0, -1)]
    rows = tap_rows(all_taps, hops * block_rows)
    return convolve(rows, received + [signal], gate, skip, group_width)


def solution(mesh):
    placed = (P(("rep", "seq"), None), P(("rep", "seq"), None), P(), P("seq", None))
    return jax.shard_map(
        body, mesh=mesh, in_specs=placed, out_specs=P(("rep", "seq"), None), check_vma=False
    )
```

```python
import functools

import jax
import jax.numpy as jnp
from jax import lax
from jax.experimental import pallas as pl
from jax.experimental.pallas import tpu as pltpu
from jax.sharding import PartitionSpec as P

TILE = 128
LANES = 128


def from_behind(shard, axis, by):
    count = lax.axis_size(axis)
    pairs = [(i, i + by) for i in range(count) if 0 <= i + by < count]
    return lax.ppermute(shard, axis, pairs)


def tap_rows(all_taps, history):
    filter_len, group_count = all_taps.shape
    flipped = all_taps.T[:, ::-1].astype(jnp.float32)
    front = jnp.zeros((group_count, TILE + history - filter_len + 1), jnp.float32)
    back = jnp.zeros((group_count, TILE - 1), jnp.float32)
    return jnp.concatenate([front, flipped, back], axis=1)


def conv_kernel(rows_ref, *refs, hops, group_width):
    blocks = refs[:hops + 1]
    gate_ref, skip_ref, out_ref = refs[hops + 1:]
    block_rows = blocks[0].shape[0]
    groups_here = rows_ref.shape[0]
    span = hops * block_rows + TILE
    sub_tiles = span // TILE
    out_tiles = block_rows // TILE
    x = jnp.concatenate([b[...] for b in blocks], axis=0)
    w = jnp.concatenate(
        [x[i * TILE: i * TILE + span] for i in range(out_tiles)], axis=1)
    lane_group = lax.broadcasted_iota(jnp.int32, w.shape, 1) % LANES // group_width
    upper = (lax.broadcasted_iota(jnp.int32, (TILE, TILE), 1)
             >= lax.broadcasted_iota(jnp.int32, (TILE, TILE), 0))
    acc = jnp.zeros((TILE, w.shape[1]), jnp.float32)
    for gg in range(groups_here):
        rolled = []
        for k in range(sub_tiles + 1):
            window = rows_ref[gg:gg + 1, k * TILE:(k + 1) * TILE]
            window = jnp.broadcast_to(window, (TILE, TILE))
            rolled.append(pltpu.roll(window, 0, 1, stride=1, stride_axis=0))
        toeplitz = jnp.concatenate(
            [jnp.where(upper, rolled[k + 1], rolled[k]) for k in range(sub_tiles)],
            axis=1).astype(jnp.bfloat16)
        masked = jnp.where(lane_group == gg, w, jnp.zeros_like(w))
        acc = acc + jnp.dot(toeplitz, masked, preferred_element_type=jnp.float32)
    conv = jnp.concatenate(
        [acc[:, i * LANES:(i + 1) * LANES] for i in range(out_tiles)], axis=0)
    cur = blocks[hops][...].astype(jnp.float32)
    mixed = gate_ref[...].astype(jnp.float32) * (conv + skip_ref[...] * cur)
    out_ref[...] = mixed.astype(out_ref.dtype)


def convolve(rows, blocks, gate, skip, group_width):
    hops = len(blocks) - 1
    block_rows, channels = gate.shape
    chunks = channels // LANES
    groups_per = LANES // group_width
    block_spec = pl.BlockSpec((block_rows, LANES), lambda c: (0, c))
    arrays, specs = [], []
    for block in blocks:
        if isinstance(block, tuple):
            arrays.append(block[0])
            specs.append(pl.BlockSpec((None, block_rows, LANES),
                                      lambda c, slot=block[1]: (slot, 0, c)))
        else:
            arrays.append(block)
            specs.append(block_spec)
    kernel = functools.partial(conv_kernel, hops=hops, group_width=group_width)
    return pl.pallas_call(
        kernel,
        grid=(chunks,),
        in_specs=[pl.BlockSpec((groups_per, rows.shape[1]), lambda c: (c, 0))]
        + specs
        + [block_spec, pl.BlockSpec((1, LANES), lambda c: (0, c))],
        out_specs=block_spec,
        out_shape=jax.ShapeDtypeStruct(gate.shape, gate.dtype),
        compiler_params=pltpu.CompilerParams(dimension_semantics=("arbitrary",)),
    )(rows, *arrays, gate, skip.reshape(1, channels))


def body(signal, gate, skip, taps):
    block_rows, channels = signal.shape
    group_count = taps.shape[1]
    group_width = channels // group_count
    all_taps = lax.all_gather(taps, "seq", axis=0, tiled=True)
    filter_len = all_taps.shape[0]
    hops = -(-(filter_len - 1) // block_rows)
    all_taps, signal = lax.optimization_barrier((all_taps, signal))
    rows = tap_rows(all_taps, hops * block_rows)
    if hops != 4 or lax.axis_size("seq") % 2:
        received = [from_behind(signal, "seq", d) for d in range(hops, 0, -1)]
        return convolve(rows, received + [signal], gate, skip, group_width)
    back_one = from_behind(signal, "seq", 2)
    back_two = from_behind(signal, "seq", 4)
    first_core = lax.axis_index("seq") % 2 == 0
    outgoing = jnp.stack([jnp.where(first_core, signal, back_one),
                          jnp.where(first_core, back_one, back_two)])
    count = lax.axis_size("seq")
    swap = [(i, i ^ 1) for i in range(count)]
    odd = lax.ppermute(outgoing, "seq", swap)
    return convolve(rows, [back_two, (odd, 1), back_one, (odd, 0), signal],
                    gate, skip, group_width)


def solution(mesh):
    placed = (P(("rep", "seq"), None), P(("rep", "seq"), None), P(), P("seq", None))
    return jax.shard_map(
        body, mesh=mesh, in_specs=placed, out_specs=P(("rep", "seq"), None), check_vma=False
    )
```

```python
import functools

import jax
import jax.numpy as jnp
from jax import lax
from jax.experimental import pallas as pl
from jax.experimental.pallas import tpu as pltpu
from jax.sharding import PartitionSpec as P

TILE = 128
LANES = 128


def from_behind(shard, axis, by):
    count = lax.axis_size(axis)
    pairs = [(i, i + by) for i in range(count) if 0 <= i + by < count]
    return lax.ppermute(shard, axis, pairs)


def tap_rows(taps, first_lag, filter_len, history):
    share, group_count = taps.shape
    flipped = taps.T[:, ::-1]
    width = history + 2 * TILE
    start = TILE + history - first_lag - share + 1
    return lax.dynamic_update_slice(
        jnp.zeros((group_count, width), taps.dtype), flipped, (0, start))


def conv_kernel(rows_ref, *refs, hops, group_width):
    blocks = refs[:hops + 1]
    gate_ref, skip_ref, out_ref = refs[hops + 1:]
    block_rows = blocks[0].shape[0]
    groups_here = rows_ref.shape[0]
    span = hops * block_rows + TILE
    sub_tiles = span // TILE
    out_tiles = block_rows // TILE
    x = jnp.concatenate([b[...] for b in blocks], axis=0)
    w = jnp.concatenate(
        [x[i * TILE: i * TILE + span] for i in range(out_tiles)], axis=1)
    lane_group = lax.broadcasted_iota(jnp.int32, w.shape, 1) % LANES // group_width
    upper = (lax.broadcasted_iota(jnp.int32, (TILE, TILE), 1)
             >= lax.broadcasted_iota(jnp.int32, (TILE, TILE), 0))
    acc = jnp.zeros((TILE, w.shape[1]), jnp.float32)
    for gg in range(groups_here):
        rolled = []
        for k in range(sub_tiles + 1):
            window = rows_ref[gg:gg + 1, k * TILE:(k + 1) * TILE]
            window = jnp.broadcast_to(window, (TILE, TILE))
            rolled.append(pltpu.roll(window, 0, 1, stride=1, stride_axis=0))
        toeplitz = jnp.concatenate(
            [jnp.where(upper, rolled[k + 1], rolled[k]) for k in range(sub_tiles)],
            axis=1).astype(jnp.bfloat16)
        masked = jnp.where(lane_group == gg, w, jnp.zeros_like(w))
        acc = acc + jnp.dot(toeplitz, masked, preferred_element_type=jnp.float32)
    conv = jnp.concatenate(
        [acc[:, i * LANES:(i + 1) * LANES] for i in range(out_tiles)], axis=0)
    cur = blocks[hops][...].astype(jnp.float32)
    mixed = gate_ref[...].astype(jnp.float32) * (conv + skip_ref[...] * cur)
    out_ref[...] = mixed.astype(out_ref.dtype)


def convolve(rows, blocks, gate, skip, group_width):
    hops = len(blocks) - 1
    block_rows, channels = gate.shape
    chunks = channels // LANES
    groups_per = LANES // group_width
    block_spec = pl.BlockSpec((block_rows, LANES), lambda c: (0, c))
    arrays, specs = [], []
    for block in blocks:
        if isinstance(block, tuple):
            arrays.append(block[0])
            specs.append(pl.BlockSpec((None, block_rows, LANES),
                                      lambda c, slot=block[1]: (slot, 0, c)))
        else:
            arrays.append(block)
            specs.append(block_spec)
    kernel = functools.partial(conv_kernel, hops=hops, group_width=group_width)
    return pl.pallas_call(
        kernel,
        grid=(chunks,),
        in_specs=[pl.BlockSpec((groups_per, rows.shape[1]), lambda c: (c, 0))]
        + specs
        + [block_spec, pl.BlockSpec((1, LANES), lambda c: (0, c))],
        out_specs=block_spec,
        out_shape=jax.ShapeDtypeStruct(gate.shape, gate.dtype),
        compiler_params=pltpu.CompilerParams(dimension_semantics=("arbitrary",)),
    )(rows, *arrays, gate, skip.reshape(1, channels))


def body(signal, gate, skip, taps):
    block_rows, channels = signal.shape
    group_count = taps.shape[1]
    group_width = channels // group_count
    share = taps.shape[0]
    filter_len = share * lax.axis_size("seq")
    hops = -(-(filter_len - 1) // block_rows)
    placed = tap_rows(taps, lax.axis_index("seq") * share, filter_len, hops * block_rows)
    placed, signal = lax.optimization_barrier((placed, signal))
    rows = lax.psum(placed, "seq").astype(jnp.float32)
    if hops != 4 or lax.axis_size("seq") % 2:
        received = [from_behind(signal, "seq", d) for d in range(hops, 0, -1)]
        return convolve(rows, received + [signal], gate, skip, group_width)
    back_one = from_behind(signal, "seq", 2)
    back_two = from_behind(signal, "seq", 4)
    first_core = lax.axis_index("seq") % 2 == 0
    outgoing = jnp.stack([jnp.where(first_core, signal, back_one),
                          jnp.where(first_core, back_one, back_two)])
    count = lax.axis_size("seq")
    swap = [(i, i ^ 1) for i in range(count)]
    odd = lax.ppermute(outgoing, "seq", swap)
    return convolve(rows, [back_two, (odd, 1), back_one, (odd, 0), signal],
                    gate, skip, group_width)


def solution(mesh):
    placed = (P(("rep", "seq"), None), P(("rep", "seq"), None), P(), P("seq", None))
    return jax.shard_map(
        body, mesh=mesh, in_specs=placed, out_specs=P(("rep", "seq"), None), check_vma=False
    )
```

```python
import functools

import jax
import jax.numpy as jnp
from jax import lax
from jax.experimental import pallas as pl
from jax.experimental.pallas import tpu as pltpu
from jax.sharding import PartitionSpec as P

TILE = 128
LANES = 128


def from_behind(shard, axis, by):
    count = lax.axis_size(axis)
    pairs = [(i, i + by) for i in range(count) if 0 <= i + by < count]
    return lax.ppermute(shard, axis, pairs)


def tap_rows(all_taps, history):
    filter_len, group_count = all_taps.shape
    flipped = all_taps.T[:, ::-1].astype(jnp.float32)
    front = jnp.zeros((group_count, TILE + history - filter_len + 1), jnp.float32)
    back = jnp.zeros((group_count, TILE - 1), jnp.float32)
    return jnp.concatenate([front, flipped, back], axis=1)


def conv_kernel(rows_ref, *refs, hops, group_width):
    blocks = refs[:hops + 1]
    gate_ref, skip_ref, out_ref = refs[hops + 1:]
    block_rows = blocks[0].shape[0]
    groups_here = rows_ref.shape[0]
    span = hops * block_rows + TILE
    sub_tiles = span // TILE
    out_tiles = block_rows // TILE
    x = jnp.concatenate([b[...] for b in blocks], axis=0)
    w = jnp.concatenate(
        [x[i * TILE: i * TILE + span] for i in range(out_tiles)], axis=1)
    lane_group = lax.broadcasted_iota(jnp.int32, w.shape, 1) % LANES // group_width
    upper = (lax.broadcasted_iota(jnp.int32, (TILE, TILE), 1)
             >= lax.broadcasted_iota(jnp.int32, (TILE, TILE), 0))
    acc = jnp.zeros((TILE, w.shape[1]), jnp.float32)
    for gg in range(groups_here):
        rolled = []
        for k in range(sub_tiles + 1):
            window = rows_ref[gg:gg + 1, k * TILE:(k + 1) * TILE]
            window = jnp.broadcast_to(window, (TILE, TILE))
            rolled.append(pltpu.roll(window, 0, 1, stride=1, stride_axis=0))
        toeplitz = jnp.concatenate(
            [jnp.where(upper, rolled[k + 1], rolled[k]) for k in range(sub_tiles)],
            axis=1).astype(jnp.bfloat16)
        masked = jnp.where(lane_group == gg, w, jnp.zeros_like(w))
        acc = acc + jnp.dot(toeplitz, masked, preferred_element_type=jnp.float32)
    conv = jnp.concatenate(
        [acc[:, i * LANES:(i + 1) * LANES] for i in range(out_tiles)], axis=0)
    cur = blocks[hops][...].astype(jnp.float32)
    mixed = gate_ref[...].astype(jnp.float32) * (conv + skip_ref[...] * cur)
    out_ref[...] = mixed.astype(out_ref.dtype)


def convolve(rows, blocks, gate, skip, group_width):
    hops = len(blocks) - 1
    block_rows, channels = gate.shape
    chunks = channels // LANES
    groups_per = LANES // group_width
    block_spec = pl.BlockSpec((block_rows, LANES), lambda c: (0, c))
    arrays, specs = [], []
    for block in blocks:
        if isinstance(block, tuple):
            arrays.append(block[0])
            specs.append(pl.BlockSpec((None, block_rows, LANES),
                                      lambda c, slot=block[1]: (slot, 0, c)))
        else:
            arrays.append(block)
            specs.append(block_spec)
    kernel = functools.partial(conv_kernel, hops=hops, group_width=group_width)
    return pl.pallas_call(
        kernel,
        grid=(chunks,),
        in_specs=[pl.BlockSpec((groups_per, rows.shape[1]), lambda c: (c, 0))]
        + specs
        + [block_spec, pl.BlockSpec((1, LANES), lambda c: (0, c))],
        out_specs=block_spec,
        out_shape=jax.ShapeDtypeStruct(gate.shape, gate.dtype),
        compiler_params=pltpu.CompilerParams(dimension_semantics=("arbitrary",)),
    )(rows, *arrays, gate, skip.reshape(1, channels))


def body(signal, gate, skip, taps):
    block_rows, channels = signal.shape
    group_count = taps.shape[1]
    group_width = channels // group_count
    filter_len = taps.shape[0] * lax.axis_size("seq")
    hops = -(-(filter_len - 1) // block_rows)
    if hops != 4 or lax.axis_size("seq") % 2:
        all_taps = lax.all_gather(taps, "seq", axis=0, tiled=True)
        rows = tap_rows(all_taps, hops * block_rows)
        received = [from_behind(signal, "seq", d) for d in range(hops, 0, -1)]
        return convolve(rows, received + [signal], gate, skip, group_width)
    back_one = from_behind(signal, "seq", 2)
    back_two = from_behind(signal, "seq", 4)
    first_core = lax.axis_index("seq") % 2 == 0
    outgoing = jnp.stack([jnp.where(first_core, signal, back_one),
                          jnp.where(first_core, back_one, back_two)])
    count = lax.axis_size("seq")
    swap = [(i, i ^ 1) for i in range(count)]
    odd = lax.ppermute(outgoing, "seq", swap)
    taps, back_one, back_two = lax.optimization_barrier((taps, back_one, back_two))
    all_taps = lax.all_gather(taps, "seq", axis=0, tiled=True)
    rows = tap_rows(all_taps, hops * block_rows)
    return convolve(rows, [back_two, (odd, 1), back_one, (odd, 0), signal],
                    gate, skip, group_width)


def solution(mesh):
    placed = (P(("rep", "seq"), None), P(("rep", "seq"), None), P(), P("seq", None))
    return jax.shard_map(
        body, mesh=mesh, in_specs=placed, out_specs=P(("rep", "seq"), None), check_vma=False
    )
```

```python
import functools

import jax
import jax.numpy as jnp
from jax import lax
from jax.experimental import pallas as pl
from jax.experimental.pallas import tpu as pltpu
from jax.sharding import PartitionSpec as P

TILE = 128
LANES = 128


def from_behind(shard, axis, by):
    count = lax.axis_size(axis)
    pairs = [(i, i + by) for i in range(count) if 0 <= i + by < count]
    return lax.ppermute(shard, axis, pairs)


def tap_rows(all_taps, history):
    filter_len, group_count = all_taps.shape
    flipped = all_taps.T[:, ::-1].astype(jnp.float32)
    front = jnp.zeros((group_count, TILE + history - filter_len + 1), jnp.float32)
    back = jnp.zeros((group_count, TILE - 1), jnp.float32)
    return jnp.concatenate([front, flipped, back], axis=1)


def conv_kernel(rows_ref, *refs, hops, group_width):
    blocks = refs[:hops + 1]
    gate_ref, skip_ref, out_ref = refs[hops + 1:]
    block_rows = blocks[0].shape[0]
    groups_here = rows_ref.shape[0]
    span = hops * block_rows + TILE
    sub_tiles = span // TILE
    out_tiles = block_rows // TILE
    x = jnp.concatenate([b[...] for b in blocks], axis=0)
    w = jnp.concatenate(
        [x[i * TILE: i * TILE + span] for i in range(out_tiles)], axis=1)
    lane_group = lax.broadcasted_iota(jnp.int32, (TILE, w.shape[1]), 1) % LANES // group_width
    upper = (lax.broadcasted_iota(jnp.int32, (TILE, TILE), 1)
             >= lax.broadcasted_iota(jnp.int32, (TILE, TILE), 0))
    acc = jnp.zeros((TILE, w.shape[1]), jnp.float32)
    for gg in range(groups_here):
        rolled = []
        for k in range(sub_tiles + 1):
            window = rows_ref[gg:gg + 1, k * TILE:(k + 1) * TILE]
            window = jnp.broadcast_to(window, (TILE, TILE))
            rolled.append(pltpu.roll(window, 0, 1, stride=1, stride_axis=0))
        toeplitz = jnp.concatenate(
            [jnp.where(upper, rolled[k + 1], rolled[k]) for k in range(sub_tiles)],
            axis=1).astype(jnp.bfloat16)
        part = jnp.dot(toeplitz, w, preferred_element_type=jnp.float32)
        acc = jnp.where(lane_group == gg, part, acc)
    conv = jnp.concatenate(
        [acc[:, i * LANES:(i + 1) * LANES] for i in range(out_tiles)], axis=0)
    cur = blocks[hops][...].astype(jnp.float32)
    mixed = gate_ref[...].astype(jnp.float32) * (conv + skip_ref[...] * cur)
    out_ref[...] = mixed.astype(out_ref.dtype)


def convolve(rows, blocks, gate, skip, group_width):
    hops = len(blocks) - 1
    block_rows, channels = gate.shape
    chunks = channels // LANES
    groups_per = LANES // group_width
    block_spec = pl.BlockSpec((block_rows, LANES), lambda c: (0, c))
    arrays, specs = [], []
    for block in blocks:
        if isinstance(block, tuple):
            arrays.append(block[0])
            specs.append(pl.BlockSpec((None, block_rows, LANES),
                                      lambda c, slot=block[1]: (slot, 0, c)))
        else:
            arrays.append(block)
            specs.append(block_spec)
    kernel = functools.partial(conv_kernel, hops=hops, group_width=group_width)
    return pl.pallas_call(
        kernel,
        grid=(chunks,),
        in_specs=[pl.BlockSpec((groups_per, rows.shape[1]), lambda c: (c, 0))]
        + specs
        + [block_spec, pl.BlockSpec((1, LANES), lambda c: (0, c))],
        out_specs=block_spec,
        out_shape=jax.ShapeDtypeStruct(gate.shape, gate.dtype),
        compiler_params=pltpu.CompilerParams(dimension_semantics=("arbitrary",)),
    )(rows, *arrays, gate, skip.reshape(1, channels))


def body(signal, gate, skip, taps):
    block_rows, channels = signal.shape
    group_count = taps.shape[1]
    group_width = channels // group_count
    all_taps = lax.all_gather(taps, "seq", axis=0, tiled=True)
    filter_len = all_taps.shape[0]
    hops = -(-(filter_len - 1) // block_rows)
    all_taps, signal = lax.optimization_barrier((all_taps, signal))
    rows = tap_rows(all_taps, hops * block_rows)
    if hops != 4 or lax.axis_size("seq") % 2:
        received = [from_behind(signal, "seq", d) for d in range(hops, 0, -1)]
        return convolve(rows, received + [signal], gate, skip, group_width)
    back_one = from_behind(signal, "seq", 2)
    back_two = from_behind(signal, "seq", 4)
    first_core = lax.axis_index("seq") % 2 == 0
    outgoing = jnp.stack([jnp.where(first_core, signal, back_one),
                          jnp.where(first_core, back_one, back_two)])
    count = lax.axis_size("seq")
    swap = [(i, i ^ 1) for i in range(count)]
    odd = lax.ppermute(outgoing, "seq", swap)
    return convolve(rows, [back_two, (odd, 1), back_one, (odd, 0), signal],
                    gate, skip, group_width)


def solution(mesh):
    placed = (P(("rep", "seq"), None), P(("rep", "seq"), None), P(), P("seq", None))
    return jax.shard_map(
        body, mesh=mesh, in_specs=placed, out_specs=P(("rep", "seq"), None), check_vma=False
    )
```

```python
import functools

import jax
import jax.numpy as jnp
from jax import lax
from jax.experimental import pallas as pl
from jax.experimental.pallas import tpu as pltpu
from jax.sharding import PartitionSpec as P

TILE = 128
LANES = 128


def from_behind(shard, axis, by):
    count = lax.axis_size(axis)
    pairs = [(i, i + by) for i in range(count) if 0 <= i + by < count]
    return lax.ppermute(shard, axis, pairs)


def tap_rows(all_taps, history):
    filter_len, group_count = all_taps.shape
    flipped = all_taps.T[:, ::-1].astype(jnp.float32)
    front = jnp.zeros((group_count, TILE + history - filter_len + 1), jnp.float32)
    back = jnp.zeros((group_count, TILE - 1), jnp.float32)
    return jnp.concatenate([front, flipped, back], axis=1)


def toeplitz(rows_ref, gg, k_lo, k_hi):
    upper = (lax.broadcasted_iota(jnp.int32, (TILE, TILE), 1)
             >= lax.broadcasted_iota(jnp.int32, (TILE, TILE), 0))
    rolled = {}
    for k in range(k_lo, k_hi + 2):
        window = jnp.broadcast_to(rows_ref[gg:gg + 1, k * TILE:(k + 1) * TILE], (TILE, TILE))
        rolled[k] = pltpu.roll(window, 0, 1, stride=1, stride_axis=0)
    return jnp.concatenate(
        [jnp.where(upper, rolled[k + 1], rolled[k]) for k in range(k_lo, k_hi + 1)],
        axis=1).astype(jnp.bfloat16)


def grouped_dot(rows_ref, w, k_lo, k_hi, group_width):
    lane_group = lax.broadcasted_iota(jnp.int32, (TILE, w.shape[1]), 1) % LANES // group_width
    acc = jnp.zeros((TILE, w.shape[1]), jnp.float32)
    for gg in range(rows_ref.shape[0]):
        part = jnp.dot(toeplitz(rows_ref, gg, k_lo, k_hi), w,
                       preferred_element_type=jnp.float32)
        acc = jnp.where(lane_group == gg, part, acc)
    return acc


def unfold(acc, out_tiles):
    return jnp.concatenate(
        [acc[:, i * LANES:(i + 1) * LANES] for i in range(out_tiles)], axis=0)


def own_kernel(rows_ref, cur_ref, out_ref, *, history_tiles, group_width):
    out_tiles = cur_ref.shape[0] // TILE
    k_lo = history_tiles - out_tiles + 1
    zero = jnp.zeros((TILE, LANES), cur_ref.dtype)
    columns = []
    for i in range(out_tiles):
        pieces = []
        for k in range(k_lo, history_tiles + 1):
            m = i + k - history_tiles
            pieces.append(cur_ref[m * TILE:(m + 1) * TILE, :] if m >= 0 else zero)
        columns.append(jnp.concatenate(pieces, axis=0))
    w = jnp.concatenate(columns, axis=1)
    acc = grouped_dot(rows_ref, w, k_lo, history_tiles, group_width)
    out_ref[...] = unfold(acc, out_tiles)


def history_kernel(rows_ref, *refs, hops, group_width):
    blocks = refs[:hops]
    own_ref, gate_ref, skip_ref, cur_ref, out_ref = refs[hops:]
    out_tiles = cur_ref.shape[0] // TILE
    x = jnp.concatenate([b[...] for b in blocks], axis=0)
    history_tiles = x.shape[0] // TILE
    zero = jnp.zeros((TILE, LANES), x.dtype)
    columns = [jnp.concatenate([x[i * TILE:]] + [zero] * i, axis=0) if i else x
               for i in range(out_tiles)]
    w = jnp.concatenate(columns, axis=1)
    acc = grouped_dot(rows_ref, w, 0, history_tiles - 1, group_width)
    conv = unfold(acc, out_tiles) + own_ref[...]
    cur = cur_ref[...].astype(jnp.float32)
    mixed = gate_ref[...].astype(jnp.float32) * (conv + skip_ref[...] * cur)
    out_ref[...] = mixed.astype(out_ref.dtype)


def own_terms(rows, signal, hops, group_width):
    block_rows, channels = signal.shape
    block_spec = pl.BlockSpec((block_rows, LANES), lambda c: (0, c))
    return pl.pallas_call(
        functools.partial(own_kernel, history_tiles=hops * block_rows // TILE,
                          group_width=group_width),
        grid=(channels // LANES,),
        in_specs=[pl.BlockSpec((LANES // group_width, rows.shape[1]), lambda c: (c, 0)),
                  block_spec],
        out_specs=block_spec,
        out_shape=jax.ShapeDtypeStruct(signal.shape, jnp.float32),
        compiler_params=pltpu.CompilerParams(dimension_semantics=("arbitrary",)),
    )(rows, signal)


def convolve(rows, blocks, own, gate, skip, signal, group_width):
    hops = len(blocks)
    block_rows, channels = gate.shape
    block_spec = pl.BlockSpec((block_rows, LANES), lambda c: (0, c))
    arrays, specs = [], []
    for block in blocks:
        if isinstance(block, tuple):
            arrays.append(block[0])
            specs.append(pl.BlockSpec((None, block_rows, LANES),
                                      lambda c, slot=block[1]: (slot, 0, c)))
        else:
            arrays.append(block)
            specs.append(block_spec)
    return pl.pallas_call(
        functools.partial(history_kernel, hops=hops, group_width=group_width),
        grid=(channels // LANES,),
        in_specs=[pl.BlockSpec((LANES // group_width, rows.shape[1]), lambda c: (c, 0))]
        + specs
        + [block_spec, block_spec, pl.BlockSpec((1, LANES), lambda c: (0, c)), block_spec],
        out_specs=block_spec,
        out_shape=jax.ShapeDtypeStruct(gate.shape, gate.dtype),
        compiler_params=pltpu.CompilerParams(dimension_semantics=("arbitrary",)),
    )(rows, *arrays, own, gate, skip.reshape(1, channels), signal)


def body(signal, gate, skip, taps):
    block_rows, channels = signal.shape
    group_count = taps.shape[1]
    group_width = channels // group_count
    all_taps = lax.all_gather(taps, "seq", axis=0, tiled=True)
    filter_len = all_taps.shape[0]
    hops = -(-(filter_len - 1) // block_rows)
    rows = tap_rows(all_taps, hops * block_rows)
    own = own_terms(rows, signal, hops, group_width)
    if hops != 4 or lax.axis_size("seq") % 2:
        received = [from_behind(signal, "seq", d) for d in range(hops, 0, -1)]
        return convolve(rows, received, own, gate, skip, signal, group_width)
    back_one = from_behind(signal, "seq", 2)
    back_two = from_behind(signal, "seq", 4)
    own, back_one, back_two = lax.optimization_barrier((own, back_one, back_two))
    first_core = lax.axis_index("seq") % 2 == 0
    outgoing = jnp.stack([jnp.where(first_core, signal, back_one),
                          jnp.where(first_core, back_one, back_two)])
    count = lax.axis_size("seq")
    swap = [(i, i ^ 1) for i in range(count)]
    odd = lax.ppermute(outgoing, "seq", swap)
    return convolve(rows, [back_two, (odd, 1), back_one, (odd, 0)], own,
                    gate, skip, signal, group_width)


def solution(mesh):
    placed = (P(("rep", "seq"), None), P(("rep", "seq"), None), P(), P("seq", None))
    return jax.shard_map(
        body, mesh=mesh, in_specs=placed, out_specs=P(("rep", "seq"), None), check_vma=False
    )
```

```python
import functools

import jax
import jax.numpy as jnp
from jax import lax
from jax.experimental import pallas as pl
from jax.experimental.pallas import tpu as pltpu
from jax.sharding import PartitionSpec as P

TILE = 128
LANES = 128


def from_behind(shard, axis, by):
    count = lax.axis_size(axis)
    pairs = [(i, i + by) for i in range(count) if 0 <= i + by < count]
    return lax.ppermute(shard, axis, pairs)


def tap_rows(all_taps, history):
    filter_len, group_count = all_taps.shape
    flipped = all_taps.T[:, ::-1].astype(jnp.float32)
    front = jnp.zeros((group_count, TILE + history - filter_len + 1), jnp.float32)
    back = jnp.zeros((group_count, TILE - 1), jnp.float32)
    return jnp.concatenate([front, flipped, back], axis=1)


def conv_kernel(rows_ref, *refs, hops, group_width):
    blocks = refs[:hops + 1]
    gate_ref, skip_ref, out_ref = refs[hops + 1:]
    block_rows = blocks[0].shape[0]
    groups_here = rows_ref.shape[0]
    span = hops * block_rows + TILE
    sub_tiles = span // TILE
    out_tiles = block_rows // TILE
    x = jnp.concatenate([b[...] for b in blocks], axis=0)
    w = jnp.concatenate(
        [x[i * TILE: i * TILE + span] for i in range(out_tiles)], axis=1)
    lane_group = lax.broadcasted_iota(jnp.int32, (TILE, w.shape[1]), 1) % LANES // group_width
    upper = (lax.broadcasted_iota(jnp.int32, (TILE, TILE), 1)
             >= lax.broadcasted_iota(jnp.int32, (TILE, TILE), 0))
    toeplitz = []
    for gg in range(groups_here):
        rolled = []
        for k in range(sub_tiles + 1):
            window = rows_ref[gg:gg + 1, k * TILE:(k + 1) * TILE]
            window = jnp.broadcast_to(window, (TILE, TILE))
            rolled.append(pltpu.roll(window, 0, 1, stride=1, stride_axis=0))
        toeplitz.append(jnp.concatenate(
            [jnp.where(upper, rolled[k + 1], rolled[k]) for k in range(sub_tiles)],
            axis=1).astype(jnp.bfloat16))
    part = jnp.dot(jnp.concatenate(toeplitz, axis=0), w, preferred_element_type=jnp.float32)
    acc = part[0:TILE]
    for gg in range(1, groups_here):
        acc = jnp.where(lane_group == gg, part[gg * TILE:(gg + 1) * TILE], acc)
    conv = jnp.concatenate(
        [acc[:, i * LANES:(i + 1) * LANES] for i in range(out_tiles)], axis=0)
    cur = blocks[hops][...].astype(jnp.float32)
    mixed = gate_ref[...].astype(jnp.float32) * (conv + skip_ref[...] * cur)
    out_ref[...] = mixed.astype(out_ref.dtype)


def convolve(rows, blocks, gate, skip, group_width):
    hops = len(blocks) - 1
    block_rows, channels = gate.shape
    chunks = channels // LANES
    groups_per = LANES // group_width
    block_spec = pl.BlockSpec((block_rows, LANES), lambda c: (0, c))
    arrays, specs = [], []
    for block in blocks:
        if isinstance(block, tuple):
            arrays.append(block[0])
            specs.append(pl.BlockSpec((None, block_rows, LANES),
                                      lambda c, slot=block[1]: (slot, 0, c)))
        else:
            arrays.append(block)
            specs.append(block_spec)
    kernel = functools.partial(conv_kernel, hops=hops, group_width=group_width)
    return pl.pallas_call(
        kernel,
        grid=(chunks,),
        in_specs=[pl.BlockSpec((groups_per, rows.shape[1]), lambda c: (c, 0))]
        + specs
        + [block_spec, pl.BlockSpec((1, LANES), lambda c: (0, c))],
        out_specs=block_spec,
        out_shape=jax.ShapeDtypeStruct(gate.shape, gate.dtype),
        compiler_params=pltpu.CompilerParams(dimension_semantics=("arbitrary",)),
    )(rows, *arrays, gate, skip.reshape(1, channels))


def body(signal, gate, skip, taps):
    block_rows, channels = signal.shape
    group_count = taps.shape[1]
    group_width = channels // group_count
    all_taps = lax.all_gather(taps, "seq", axis=0, tiled=True)
    filter_len = all_taps.shape[0]
    hops = -(-(filter_len - 1) // block_rows)
    all_taps, signal = lax.optimization_barrier((all_taps, signal))
    rows = tap_rows(all_taps, hops * block_rows)
    if hops != 4 or lax.axis_size("seq") % 2:
        received = [from_behind(signal, "seq", d) for d in range(hops, 0, -1)]
        return convolve(rows, received + [signal], gate, skip, group_width)
    back_one = from_behind(signal, "seq", 2)
    back_two = from_behind(signal, "seq", 4)
    first_core = lax.axis_index("seq") % 2 == 0
    outgoing = jnp.stack([jnp.where(first_core, signal, back_one),
                          jnp.where(first_core, back_one, back_two)])
    count = lax.axis_size("seq")
    swap = [(i, i ^ 1) for i in range(count)]
    odd = lax.ppermute(outgoing, "seq", swap)
    return convolve(rows, [back_two, (odd, 1), back_one, (odd, 0), signal],
                    gate, skip, group_width)


def solution(mesh):
    placed = (P(("rep", "seq"), None), P(("rep", "seq"), None), P(), P("seq", None))
    return jax.shard_map(
        body, mesh=mesh, in_specs=placed, out_specs=P(("rep", "seq"), None), check_vma=False
    )
```

```python
import functools

import jax
import jax.numpy as jnp
from jax import lax
from jax.experimental import pallas as pl
from jax.experimental.pallas import tpu as pltpu
from jax.sharding import PartitionSpec as P

TILE = 128
LANES = 128


def from_behind(shard, axis, by):
    count = lax.axis_size(axis)
    pairs = [(i, i + by) for i in range(count) if 0 <= i + by < count]
    return lax.ppermute(shard, axis, pairs)


def tap_rows(all_taps, history):
    filter_len, group_count = all_taps.shape
    flipped = all_taps.T[:, ::-1].astype(jnp.float32)
    front = jnp.zeros((group_count, TILE + history - filter_len + 1), jnp.float32)
    back = jnp.zeros((group_count, TILE - 1), jnp.float32)
    return jnp.concatenate([front, flipped, back], axis=1)


def conv_kernel(rows_ref, *refs, hops, group_width):
    blocks = refs[:hops + 1]
    gate_ref, skip_ref, out_ref = refs[hops + 1:]
    block_rows = blocks[0].shape[0]
    groups_here = rows_ref.shape[0]
    span = hops * block_rows + TILE
    sub_tiles = span // TILE
    out_tiles = block_rows // TILE
    x = jnp.concatenate([b[...] for b in blocks], axis=0)
    w = jnp.concatenate(
        [x[i * TILE: i * TILE + span] for i in range(out_tiles)], axis=1)
    lane_group = lax.broadcasted_iota(jnp.int32, (TILE, w.shape[1]), 1) % LANES // group_width
    upper = (lax.broadcasted_iota(jnp.int32, (TILE, TILE), 1)
             >= lax.broadcasted_iota(jnp.int32, (TILE, TILE), 0))
    acc = jnp.zeros((TILE, w.shape[1]), jnp.float32)
    for gg in range(groups_here):
        rolled = []
        for k in range(sub_tiles + 1):
            window = rows_ref[gg:gg + 1, k * TILE:(k + 1) * TILE]
            window = jnp.broadcast_to(window, (TILE, TILE))
            rolled.append(pltpu.roll(window, 0, 1, stride=1, stride_axis=0))
        toeplitz = jnp.concatenate(
            [jnp.where(upper, rolled[k + 1], rolled[k]) for k in range(sub_tiles)],
            axis=1).astype(jnp.bfloat16)
        part = jnp.dot(toeplitz, w, preferred_element_type=jnp.float32)
        acc = jnp.where(lane_group == gg, part, acc)
    conv = jnp.concatenate(
        [acc[:, i * LANES:(i + 1) * LANES] for i in range(out_tiles)], axis=0)
    cur = blocks[hops][...].astype(jnp.float32)
    mixed = gate_ref[...].astype(jnp.float32) * (conv + skip_ref[...] * cur)
    out_ref[...] = mixed.astype(out_ref.dtype)


def convolve(rows, blocks, gate, skip, group_width):
    hops = len(blocks) - 1
    block_rows, channels = gate.shape
    chunks = channels // LANES
    groups_per = LANES // group_width
    block_spec = pl.BlockSpec((block_rows, LANES), lambda c: (0, c))
    arrays, specs = [], []
    for block in blocks:
        if isinstance(block, tuple):
            arrays.append(block[0])
            specs.append(pl.BlockSpec((None, block_rows, LANES),
                                      lambda c, slot=block[1]: (slot, 0, c)))
        else:
            arrays.append(block)
            specs.append(block_spec)
    kernel = functools.partial(conv_kernel, hops=hops, group_width=group_width)
    return pl.pallas_call(
        kernel,
        grid=(chunks,),
        in_specs=[pl.BlockSpec((groups_per, rows.shape[1]), lambda c: (c, 0))]
        + specs
        + [block_spec, pl.BlockSpec((1, LANES), lambda c: (0, c))],
        out_specs=block_spec,
        out_shape=jax.ShapeDtypeStruct(gate.shape, gate.dtype),
        compiler_params=pltpu.CompilerParams(dimension_semantics=("arbitrary",)),
    )(rows, *arrays, gate, skip.reshape(1, channels))


def body(signal, gate, skip, taps):
    block_rows, channels = signal.shape
    group_count = taps.shape[1]
    group_width = channels // group_count
    count = lax.axis_size("seq")
    spread = jnp.concatenate([taps] * count, axis=0)
    all_taps = lax.all_to_all(spread, "seq", 0, 0, tiled=True)
    filter_len = all_taps.shape[0]
    hops = -(-(filter_len - 1) // block_rows)
    all_taps, signal = lax.optimization_barrier((all_taps, signal))
    rows = tap_rows(all_taps, hops * block_rows)
    if hops != 4 or lax.axis_size("seq") % 2:
        received = [from_behind(signal, "seq", d) for d in range(hops, 0, -1)]
        return convolve(rows, received + [signal], gate, skip, group_width)
    back_one = from_behind(signal, "seq", 2)
    back_two = from_behind(signal, "seq", 4)
    first_core = lax.axis_index("seq") % 2 == 0
    outgoing = jnp.stack([jnp.where(first_core, signal, back_one),
                          jnp.where(first_core, back_one, back_two)])
    swap = [(i, i ^ 1) for i in range(count)]
    odd = lax.ppermute(outgoing, "seq", swap)
    return convolve(rows, [back_two, (odd, 1), back_one, (odd, 0), signal],
                    gate, skip, group_width)


def solution(mesh):
    placed = (P(("rep", "seq"), None), P(("rep", "seq"), None), P(), P("seq", None))
    return jax.shard_map(
        body, mesh=mesh, in_specs=placed, out_specs=P(("rep", "seq"), None), check_vma=False
    )
```

```python
import functools

import jax
import jax.numpy as jnp
from jax import lax
from jax.experimental import pallas as pl
from jax.experimental.pallas import tpu as pltpu
from jax.sharding import PartitionSpec as P

TILE = 128
LANES = 128
STEP = 64


def from_behind(shard, axis, by):
    count = lax.axis_size(axis)
    pairs = [(i, i + by) for i in range(count) if 0 <= i + by < count]
    return lax.ppermute(shard, axis, pairs)


def tap_rows(all_taps, history):
    filter_len, group_count = all_taps.shape
    flipped = all_taps.T[:, ::-1].astype(jnp.float32)
    front = jnp.zeros((group_count, TILE + history - filter_len + 1), jnp.float32)
    back = jnp.zeros((group_count, TILE - 1), jnp.float32)
    return jnp.concatenate([front, flipped, back], axis=1)


def conv_kernel(rows_ref, *refs, hops, group_width):
    blocks = refs[:hops + 1]
    gate_ref, skip_ref, out_ref = refs[hops + 1:]
    block_rows = blocks[0].shape[0]
    groups_here = rows_ref.shape[0]
    out_tiles = block_rows // STEP
    span = hops * block_rows + STEP
    col_blocks = -(-span // TILE)
    width = col_blocks * TILE
    x = jnp.concatenate([b[...] for b in blocks], axis=0)
    pad = (out_tiles - 1) * STEP + width - x.shape[0]
    x = jnp.concatenate([x, jnp.zeros((pad, x.shape[1]), x.dtype)], axis=0)
    w = jnp.concatenate(
        [x[i * STEP: i * STEP + width] for i in range(out_tiles)], axis=1)
    lane_group = lax.broadcasted_iota(jnp.int32, (STEP, w.shape[1]), 1) % LANES // group_width
    upper = (lax.broadcasted_iota(jnp.int32, (STEP, TILE), 1)
             >= lax.broadcasted_iota(jnp.int32, (STEP, TILE), 0))
    acc = jnp.zeros((STEP, w.shape[1]), jnp.float32)
    for gg in range(groups_here):
        rolled = []
        for k in range(col_blocks + 1):
            window = rows_ref[gg:gg + 1, k * TILE:(k + 1) * TILE]
            window = jnp.broadcast_to(window, (STEP, TILE))
            rolled.append(pltpu.roll(window, 0, 1, stride=1, stride_axis=0))
        toeplitz = jnp.concatenate(
            [jnp.where(upper, rolled[k + 1], rolled[k]) for k in range(col_blocks)],
            axis=1).astype(jnp.bfloat16)
        part = jnp.dot(toeplitz, w, preferred_element_type=jnp.float32)
        acc = jnp.where(lane_group == gg, part, acc)
    conv = jnp.concatenate(
        [acc[:, i * LANES:(i + 1) * LANES] for i in range(out_tiles)], axis=0)
    cur = blocks[hops][...].astype(jnp.float32)
    mixed = gate_ref[...].astype(jnp.float32) * (conv + skip_ref[...] * cur)
    out_ref[...] = mixed.astype(out_ref.dtype)


def convolve(rows, blocks, gate, skip, group_width):
    hops = len(blocks) - 1
    block_rows, channels = gate.shape
    chunks = channels // LANES
    groups_per = LANES // group_width
    block_spec = pl.BlockSpec((block_rows, LANES), lambda c: (0, c))
    arrays, specs = [], []
    for block in blocks:
        if isinstance(block, tuple):
            arrays.append(block[0])
            specs.append(pl.BlockSpec((None, block_rows, LANES),
                                      lambda c, slot=block[1]: (slot, 0, c)))
        else:
            arrays.append(block)
            specs.append(block_spec)
    kernel = functools.partial(conv_kernel, hops=hops, group_width=group_width)
    return pl.pallas_call(
        kernel,
        grid=(chunks,),
        in_specs=[pl.BlockSpec((groups_per, rows.shape[1]), lambda c: (c, 0))]
        + specs
        + [block_spec, pl.BlockSpec((1, LANES), lambda c: (0, c))],
        out_specs=block_spec,
        out_shape=jax.ShapeDtypeStruct(gate.shape, gate.dtype),
        compiler_params=pltpu.CompilerParams(dimension_semantics=("arbitrary",)),
    )(rows, *arrays, gate, skip.reshape(1, channels))


def body(signal, gate, skip, taps):
    block_rows, channels = signal.shape
    group_count = taps.shape[1]
    group_width = channels // group_count
    all_taps = lax.all_gather(taps, "seq", axis=0, tiled=True)
    filter_len = all_taps.shape[0]
    hops = -(-(filter_len - 1) // block_rows)
    all_taps, signal = lax.optimization_barrier((all_taps, signal))
    rows = tap_rows(all_taps, hops * block_rows)
    if hops != 4 or lax.axis_size("seq") % 2:
        received = [from_behind(signal, "seq", d) for d in range(hops, 0, -1)]
        return convolve(rows, received + [signal], gate, skip, group_width)
    back_one = from_behind(signal, "seq", 2)
    back_two = from_behind(signal, "seq", 4)
    first_core = lax.axis_index("seq") % 2 == 0
    outgoing = jnp.stack([jnp.where(first_core, signal, back_one),
                          jnp.where(first_core, back_one, back_two)])
    count = lax.axis_size("seq")
    swap = [(i, i ^ 1) for i in range(count)]
    odd = lax.ppermute(outgoing, "seq", swap)
    return convolve(rows, [back_two, (odd, 1), back_one, (odd, 0), signal],
                    gate, skip, group_width)


def solution(mesh):
    placed = (P(("rep", "seq"), None), P(("rep", "seq"), None), P(), P("seq", None))
    return jax.shard_map(
        body, mesh=mesh, in_specs=placed, out_specs=P(("rep", "seq"), None), check_vma=False
    )
```

```python
import functools

import jax
import jax.numpy as jnp
from jax import lax
from jax.experimental import pallas as pl
from jax.experimental.pallas import tpu as pltpu
from jax.sharding import PartitionSpec as P

TILE = 128
LANES = 128


def from_behind(shard, axis, by):
    count = lax.axis_size(axis)
    pairs = [(i, i + by) for i in range(count) if 0 <= i + by < count]
    return lax.ppermute(shard, axis, pairs)


def tap_rows(all_taps, history):
    filter_len, group_count = all_taps.shape
    flipped = all_taps.T[:, ::-1].astype(jnp.float32)
    front = jnp.zeros((group_count, TILE + history - filter_len + 1), jnp.float32)
    back = jnp.zeros((group_count, TILE - 1), jnp.float32)
    return jnp.concatenate([front, flipped, back], axis=1)


def conv_kernel(rows_ref, *refs, hops, group_width):
    blocks = refs[:hops + 1]
    gate_ref, skip_ref, out_ref = refs[hops + 1:]
    block_rows = blocks[0].shape[0]
    groups_here = rows_ref.shape[0]
    span = hops * block_rows + TILE
    sub_tiles = span // TILE
    out_tiles = block_rows // TILE
    x = jnp.concatenate([b[...] for b in blocks], axis=0)
    w = jnp.concatenate(
        [x[i * TILE: i * TILE + span] for i in range(out_tiles)], axis=1)
    lane_group = lax.broadcasted_iota(jnp.int32, (TILE, w.shape[1]), 1) % LANES // group_width
    upper = (lax.broadcasted_iota(jnp.int32, (TILE, TILE), 1)
             >= lax.broadcasted_iota(jnp.int32, (TILE, TILE), 0))
    acc = jnp.zeros((TILE, w.shape[1]), jnp.float32)
    for gg in range(groups_here):
        rolled = []
        for k in range(sub_tiles + 1):
            window = rows_ref[gg:gg + 1, k * TILE:(k + 1) * TILE]
            window = jnp.broadcast_to(window, (TILE, TILE))
            rolled.append(pltpu.roll(window, 0, 1, stride=1, stride_axis=0))
        toeplitz = jnp.concatenate(
            [jnp.where(upper, rolled[k + 1], rolled[k]) for k in range(sub_tiles)],
            axis=1).astype(jnp.bfloat16)
        part = jnp.dot(toeplitz, w, preferred_element_type=jnp.float32)
        acc = jnp.where(lane_group == gg, part, acc)
    conv = jnp.concatenate(
        [acc[:, i * LANES:(i + 1) * LANES] for i in range(out_tiles)], axis=0)
    cur = blocks[hops][...].astype(jnp.float32)
    mixed = gate_ref[...].astype(jnp.float32) * (conv + skip_ref[...] * cur)
    out_ref[...] = mixed.astype(out_ref.dtype)


def convolve(rows, blocks, gate, skip, group_width):
    hops = len(blocks) - 1
    block_rows, channels = gate.shape
    chunks = channels // LANES
    groups_per = LANES // group_width
    block_spec = pl.BlockSpec((block_rows, LANES), lambda c: (0, c))
    arrays, specs = [], []
    for block in blocks:
        if isinstance(block, tuple):
            arrays.append(block[0])
            specs.append(pl.BlockSpec((None, block_rows, LANES),
                                      lambda c, slot=block[1]: (slot, 0, c)))
        else:
            arrays.append(block)
            specs.append(block_spec)
    kernel = functools.partial(conv_kernel, hops=hops, group_width=group_width)
    return pl.pallas_call(
        kernel,
        grid=(chunks,),
        in_specs=[pl.BlockSpec((groups_per, rows.shape[1]), lambda c: (c, 0))]
        + specs
        + [block_spec, pl.BlockSpec((1, LANES), lambda c: (0, c))],
        out_specs=block_spec,
        out_shape=jax.ShapeDtypeStruct(gate.shape, gate.dtype),
        compiler_params=pltpu.CompilerParams(dimension_semantics=("arbitrary",)),
    )(rows, *arrays, gate, skip.reshape(1, channels))


def body(signal, gate, skip, taps):
    block_rows, channels = signal.shape
    group_count = taps.shape[1]
    group_width = channels // group_count
    all_taps = lax.all_gather(taps, "seq", axis=0, tiled=True)
    filter_len = all_taps.shape[0]
    hops = -(-(filter_len - 1) // block_rows)
    all_taps, signal = lax.optimization_barrier((all_taps, signal))
    rows = tap_rows(all_taps, hops * block_rows)
    if hops != 4 or lax.axis_size("seq") % 2:
        received = [from_behind(signal, "seq", d) for d in range(hops, 0, -1)]
        return convolve(rows, received + [signal], gate, skip, group_width)
    count = lax.axis_size("seq")
    if count % 4:
        back_one = from_behind(signal, "seq", 2)
        back_two = from_behind(signal, "seq", 4)
    else:
        half = block_rows // 2
        first = from_behind(signal[:half], "seq", 4)
        first, rest = lax.optimization_barrier((first, signal[half:]))
        second = from_behind(rest, "seq", 4)
        back_two = jnp.concatenate([first, second], axis=0)
        up = [(i, i + 2) for i in range(count) if (i // 2) % 2 == 0]
        down = [(i, i - 2) for i in range(count) if (i // 2) % 2 == 1]
        direct = lax.ppermute(signal, "seq", up)
        relayed = jnp.concatenate([lax.ppermute(first, "seq", down),
                                   lax.ppermute(second, "seq", down)], axis=0)
        odd_chip = (lax.axis_index("seq") // 2) % 2 == 1
        back_one = jnp.where(odd_chip, direct, relayed)
    first_core = lax.axis_index("seq") % 2 == 0
    outgoing = jnp.stack([jnp.where(first_core, signal, back_one),
                          jnp.where(first_core, back_one, back_two)])
    swap = [(i, i ^ 1) for i in range(count)]
    odd = lax.ppermute(outgoing, "seq", swap)
    return convolve(rows, [back_two, (odd, 1), back_one, (odd, 0), signal],
                    gate, skip, group_width)


def solution(mesh):
    placed = (P(("rep", "seq"), None), P(("rep", "seq"), None), P(), P("seq", None))
    return jax.shard_map(
        body, mesh=mesh, in_specs=placed, out_specs=P(("rep", "seq"), None), check_vma=False
    )
```

```python
import functools

import jax
import jax.numpy as jnp
from jax import lax
from jax.experimental import pallas as pl
from jax.experimental.pallas import tpu as pltpu
from jax.sharding import PartitionSpec as P

TILE = 128
LANES = 128


def from_behind(shard, axis, by):
    count = lax.axis_size(axis)
    pairs = [(i, i + by) for i in range(count) if 0 <= i + by < count]
    return lax.ppermute(shard, axis, pairs)


def tap_rows(all_taps, history):
    filter_len, group_count = all_taps.shape
    flipped = all_taps.T[:, ::-1].astype(jnp.float32)
    front = jnp.zeros((group_count, TILE + history - filter_len + 1), jnp.float32)
    back = jnp.zeros((group_count, TILE - 1), jnp.float32)
    return jnp.concatenate([front, flipped, back], axis=1)


def conv_kernel(rows_ref, *refs, hops, group_width):
    blocks = refs[:hops + 1]
    gate_ref, skip_ref, out_ref = refs[hops + 1:]
    block_rows = blocks[0].shape[0]
    groups_here = LANES // group_width
    span = hops * block_rows + TILE
    sub_tiles = span // TILE
    out_tiles = block_rows // TILE
    upper = (lax.broadcasted_iota(jnp.int32, (TILE, TILE), 1)
             >= lax.broadcasted_iota(jnp.int32, (TILE, TILE), 0))
    lane_group = lax.broadcasted_iota(jnp.int32, (TILE, out_tiles * LANES), 1) % LANES // group_width
    for sub in range(blocks[0].shape[1] // LANES):
        lanes = slice(sub * LANES, (sub + 1) * LANES)
        x = jnp.concatenate([b[:, lanes] for b in blocks], axis=0)
        w = jnp.concatenate(
            [x[i * TILE: i * TILE + span] for i in range(out_tiles)], axis=1)
        acc = jnp.zeros((TILE, w.shape[1]), jnp.float32)
        for gg in range(groups_here):
            row = sub * groups_here + gg
            rolled = []
            for k in range(sub_tiles + 1):
                window = rows_ref[row:row + 1, k * TILE:(k + 1) * TILE]
                window = jnp.broadcast_to(window, (TILE, TILE))
                rolled.append(pltpu.roll(window, 0, 1, stride=1, stride_axis=0))
            toeplitz = jnp.concatenate(
                [jnp.where(upper, rolled[k + 1], rolled[k]) for k in range(sub_tiles)],
                axis=1).astype(jnp.bfloat16)
            part = jnp.dot(toeplitz, w, preferred_element_type=jnp.float32)
            acc = jnp.where(lane_group == gg, part, acc)
        conv = jnp.concatenate(
            [acc[:, i * LANES:(i + 1) * LANES] for i in range(out_tiles)], axis=0)
        cur = blocks[hops][:, lanes].astype(jnp.float32)
        mixed = gate_ref[:, lanes].astype(jnp.float32) * (conv + skip_ref[:, lanes] * cur)
        out_ref[:, lanes] = mixed.astype(out_ref.dtype)


def convolve(rows, blocks, gate, skip, group_width):
    hops = len(blocks) - 1
    block_rows, channels = gate.shape
    width = 2 * LANES if channels % (2 * LANES) == 0 else LANES
    chunks = channels // width
    groups_per = width // group_width
    block_spec = pl.BlockSpec((block_rows, width), lambda c: (0, c))
    arrays, specs = [], []
    for block in blocks:
        if isinstance(block, tuple):
            arrays.append(block[0])
            specs.append(pl.BlockSpec((None, block_rows, width),
                                      lambda c, slot=block[1]: (slot, 0, c)))
        else:
            arrays.append(block)
            specs.append(block_spec)
    kernel = functools.partial(conv_kernel, hops=hops, group_width=group_width)
    return pl.pallas_call(
        kernel,
        grid=(chunks,),
        in_specs=[pl.BlockSpec((groups_per, rows.shape[1]), lambda c: (c, 0))]
        + specs
        + [block_spec, pl.BlockSpec((1, width), lambda c: (0, c))],
        out_specs=block_spec,
        out_shape=jax.ShapeDtypeStruct(gate.shape, gate.dtype),
        compiler_params=pltpu.CompilerParams(dimension_semantics=("arbitrary",)),
    )(rows, *arrays, gate, skip.reshape(1, channels))


def body(signal, gate, skip, taps):
    block_rows, channels = signal.shape
    group_count = taps.shape[1]
    group_width = channels // group_count
    all_taps = lax.all_gather(taps, "seq", axis=0, tiled=True)
    filter_len = all_taps.shape[0]
    hops = -(-(filter_len - 1) // block_rows)
    all_taps, signal = lax.optimization_barrier((all_taps, signal))
    rows = tap_rows(all_taps, hops * block_rows)
    if hops != 4 or lax.axis_size("seq") % 2:
        received = [from_behind(signal, "seq", d) for d in range(hops, 0, -1)]
        return convolve(rows, received + [signal], gate, skip, group_width)
    back_one = from_behind(signal, "seq", 2)
    back_two = from_behind(signal, "seq", 4)
    first_core = lax.axis_index("seq") % 2 == 0
    outgoing = jnp.stack([jnp.where(first_core, signal, back_one),
                          jnp.where(first_core, back_one, back_two)])
    count = lax.axis_size("seq")
    swap = [(i, i ^ 1) for i in range(count)]
    odd = lax.ppermute(outgoing, "seq", swap)
    return convolve(rows, [back_two, (odd, 1), back_one, (odd, 0), signal],
                    gate, skip, group_width)


def solution(mesh):
    placed = (P(("rep", "seq"), None), P(("rep", "seq"), None), P(), P("seq", None))
    return jax.shard_map(
        body, mesh=mesh, in_specs=placed, out_specs=P(("rep", "seq"), None), check_vma=False
    )
```

```python
import functools

import jax
import jax.numpy as jnp
from jax import lax
from jax.experimental import pallas as pl
from jax.experimental.pallas import tpu as pltpu
from jax.sharding import PartitionSpec as P

TILE = 128
LANES = 128


def from_behind(shard, axis, by):
    count = lax.axis_size(axis)
    pairs = [(i, i + by) for i in range(count) if 0 <= i + by < count]
    return lax.ppermute(shard, axis, pairs)


def tap_rows(all_taps, history):
    filter_len, group_count = all_taps.shape
    flipped = all_taps.T[:, ::-1].astype(jnp.float32)
    front = jnp.zeros((group_count, TILE + history - filter_len + 1), jnp.float32)
    back = jnp.zeros((group_count, TILE - 1), jnp.float32)
    return jnp.concatenate([front, flipped, back], axis=1)


def conv_kernel(rows_ref, *refs, hops, group_width):
    blocks = refs[:hops + 1]
    gate_ref, skip_ref, out_ref = refs[hops + 1:]
    block_rows = blocks[0].shape[0]
    groups_here = LANES // group_width
    span = hops * block_rows + TILE
    sub_tiles = span // TILE
    out_tiles = block_rows // TILE
    upper = (lax.broadcasted_iota(jnp.int32, (TILE, TILE), 1)
             >= lax.broadcasted_iota(jnp.int32, (TILE, TILE), 0))
    lane_group = lax.broadcasted_iota(jnp.int32, (TILE, out_tiles * LANES), 1) % LANES // group_width
    for sub in range(blocks[0].shape[1] // LANES):
        lanes = slice(sub * LANES, (sub + 1) * LANES)
        x = jnp.concatenate([b[:, lanes] for b in blocks], axis=0)
        w = jnp.concatenate(
            [x[i * TILE: i * TILE + span] for i in range(out_tiles)], axis=1)
        acc = jnp.zeros((TILE, w.shape[1]), jnp.float32)
        for gg in range(groups_here):
            row = sub * groups_here + gg
            rolled = []
            for k in range(sub_tiles + 1):
                window = rows_ref[row:row + 1, k * TILE:(k + 1) * TILE]
                window = jnp.broadcast_to(window, (TILE, TILE))
                rolled.append(pltpu.roll(window, 0, 1, stride=1, stride_axis=0))
            toeplitz = jnp.concatenate(
                [jnp.where(upper, rolled[k + 1], rolled[k]) for k in range(sub_tiles)],
                axis=1).astype(jnp.bfloat16)
            part = jnp.dot(toeplitz, w, preferred_element_type=jnp.float32)
            acc = jnp.where(lane_group == gg, part, acc)
        conv = jnp.concatenate(
            [acc[:, i * LANES:(i + 1) * LANES] for i in range(out_tiles)], axis=0)
        cur = blocks[hops][:, lanes].astype(jnp.float32)
        mixed = gate_ref[:, lanes].astype(jnp.float32) * (conv + skip_ref[:, lanes] * cur)
        out_ref[:, lanes] = mixed.astype(out_ref.dtype)


def convolve(rows, blocks, gate, skip, group_width):
    hops = len(blocks) - 1
    block_rows, channels = gate.shape
    subs = next(n for n in (4, 2, 1) if channels % (n * LANES) == 0)
    width = subs * LANES
    chunks = channels // width
    groups_per = width // group_width
    block_spec = pl.BlockSpec((block_rows, width), lambda c: (0, c))
    arrays, specs = [], []
    for block in blocks:
        if isinstance(block, tuple):
            arrays.append(block[0])
            specs.append(pl.BlockSpec((None, block_rows, width),
                                      lambda c, slot=block[1]: (slot, 0, c)))
        else:
            arrays.append(block)
            specs.append(block_spec)
    kernel = functools.partial(conv_kernel, hops=hops, group_width=group_width)
    return pl.pallas_call(
        kernel,
        grid=(chunks,),
        in_specs=[pl.BlockSpec((groups_per, rows.shape[1]), lambda c: (c, 0))]
        + specs
        + [block_spec, pl.BlockSpec((1, width), lambda c: (0, c))],
        out_specs=block_spec,
        out_shape=jax.ShapeDtypeStruct(gate.shape, gate.dtype),
        compiler_params=pltpu.CompilerParams(dimension_semantics=("arbitrary",)),
    )(rows, *arrays, gate, skip.reshape(1, channels))


def body(signal, gate, skip, taps):
    block_rows, channels = signal.shape
    group_count = taps.shape[1]
    group_width = channels // group_count
    all_taps = lax.all_gather(taps, "seq", axis=0, tiled=True)
    filter_len = all_taps.shape[0]
    hops = -(-(filter_len - 1) // block_rows)
    all_taps, signal = lax.optimization_barrier((all_taps, signal))
    rows = tap_rows(all_taps, hops * block_rows)
    if hops != 4 or lax.axis_size("seq") % 2:
        received = [from_behind(signal, "seq", d) for d in range(hops, 0, -1)]
        return convolve(rows, received + [signal], gate, skip, group_width)
    back_one = from_behind(signal, "seq", 2)
    back_two = from_behind(signal, "seq", 4)
    first_core = lax.axis_index("seq") % 2 == 0
    outgoing = jnp.stack([jnp.where(first_core, signal, back_one),
                          jnp.where(first_core, back_one, back_two)])
    count = lax.axis_size("seq")
    swap = [(i, i ^ 1) for i in range(count)]
    odd = lax.ppermute(outgoing, "seq", swap)
    return convolve(rows, [back_two, (odd, 1), back_one, (odd, 0), signal],
                    gate, skip, group_width)


def solution(mesh):
    placed = (P(("rep", "seq"), None), P(("rep", "seq"), None), P(), P("seq", None))
    return jax.shard_map(
        body, mesh=mesh, in_specs=placed, out_specs=P(("rep", "seq"), None), check_vma=False
    )
```

```python
import functools

import jax
import jax.numpy as jnp
from jax import lax
from jax.experimental import pallas as pl
from jax.experimental.pallas import tpu as pltpu
from jax.sharding import PartitionSpec as P

TILE = 128
LANES = 128


def from_behind(shard, axis, by):
    count = lax.axis_size(axis)
    pairs = [(i, i + by) for i in range(count) if 0 <= i + by < count]
    return lax.ppermute(shard, axis, pairs)


def tap_rows(all_taps, history):
    filter_len, group_count = all_taps.shape
    flipped = all_taps.T[:, ::-1].astype(jnp.float32)
    front = jnp.zeros((group_count, TILE + history - filter_len + 1), jnp.float32)
    back = jnp.zeros((group_count, TILE - 1), jnp.float32)
    return jnp.concatenate([front, flipped, back], axis=1)


def conv_kernel(rows_ref, *refs, hops, group_width):
    blocks = refs[:hops + 1]
    gate_ref, skip_ref, out_ref = refs[hops + 1:]
    block_rows = blocks[0].shape[0]
    groups_here = LANES // group_width
    span = hops * block_rows + TILE
    sub_tiles = span // TILE
    out_tiles = block_rows // TILE
    upper = (lax.broadcasted_iota(jnp.int32, (TILE, TILE), 1)
             >= lax.broadcasted_iota(jnp.int32, (TILE, TILE), 0))
    lane_group = lax.broadcasted_iota(jnp.int32, (TILE, out_tiles * LANES), 1) % LANES // group_width
    for sub in range(blocks[0].shape[1] // LANES):
        lanes = slice(sub * LANES, (sub + 1) * LANES)
        x = jnp.concatenate([b[:, lanes] for b in blocks], axis=0)
        w = jnp.concatenate(
            [x[i * TILE: i * TILE + span] for i in range(out_tiles)], axis=1)
        acc = jnp.zeros((TILE, w.shape[1]), jnp.float32)
        for gg in range(groups_here):
            row = sub * groups_here + gg
            rolled = []
            for k in range(sub_tiles + 1):
                window = rows_ref[row:row + 1, k * TILE:(k + 1) * TILE]
                window = jnp.broadcast_to(window, (TILE, TILE))
                rolled.append(pltpu.roll(window, 0, 1, stride=1, stride_axis=0))
            toeplitz = jnp.concatenate(
                [jnp.where(upper, rolled[k + 1], rolled[k]) for k in range(sub_tiles)],
                axis=1).astype(jnp.bfloat16)
            part = jnp.dot(toeplitz, w, preferred_element_type=jnp.float32)
            acc = jnp.where(lane_group == gg, part, acc)
        conv = jnp.concatenate(
            [acc[:, i * LANES:(i + 1) * LANES] for i in range(out_tiles)], axis=0)
        cur = blocks[hops][:, lanes].astype(jnp.float32)
        mixed = gate_ref[:, lanes].astype(jnp.float32) * (conv + skip_ref[:, lanes] * cur)
        out_ref[:, lanes] = mixed.astype(out_ref.dtype)


def convolve(rows, blocks, gate, skip, group_width):
    hops = len(blocks) - 1
    block_rows, channels = gate.shape
    subs = next(n for n in (8, 4, 2, 1) if channels % (n * LANES) == 0)
    width = subs * LANES
    chunks = channels // width
    groups_per = width // group_width
    block_spec = pl.BlockSpec((block_rows, width), lambda c: (0, c))
    arrays, specs = [], []
    for block in blocks:
        if isinstance(block, tuple):
            arrays.append(block[0])
            specs.append(pl.BlockSpec((None, block_rows, width),
                                      lambda c, slot=block[1]: (slot, 0, c)))
        else:
            arrays.append(block)
            specs.append(block_spec)
    kernel = functools.partial(conv_kernel, hops=hops, group_width=group_width)
    return pl.pallas_call(
        kernel,
        grid=(chunks,),
        in_specs=[pl.BlockSpec((groups_per, rows.shape[1]), lambda c: (c, 0))]
        + specs
        + [block_spec, pl.BlockSpec((1, width), lambda c: (0, c))],
        out_specs=block_spec,
        out_shape=jax.ShapeDtypeStruct(gate.shape, gate.dtype),
        compiler_params=pltpu.CompilerParams(dimension_semantics=("arbitrary",)),
    )(rows, *arrays, gate, skip.reshape(1, channels))


def body(signal, gate, skip, taps):
    block_rows, channels = signal.shape
    group_count = taps.shape[1]
    group_width = channels // group_count
    all_taps = lax.all_gather(taps, "seq", axis=0, tiled=True)
    filter_len = all_taps.shape[0]
    hops = -(-(filter_len - 1) // block_rows)
    all_taps, signal = lax.optimization_barrier((all_taps, signal))
    rows = tap_rows(all_taps, hops * block_rows)
    if hops != 4 or lax.axis_size("seq") % 2:
        received = [from_behind(signal, "seq", d) for d in range(hops, 0, -1)]
        return convolve(rows, received + [signal], gate, skip, group_width)
    back_one = from_behind(signal, "seq", 2)
    back_two = from_behind(signal, "seq", 4)
    first_core = lax.axis_index("seq") % 2 == 0
    outgoing = jnp.stack([jnp.where(first_core, signal, back_one),
                          jnp.where(first_core, back_one, back_two)])
    count = lax.axis_size("seq")
    swap = [(i, i ^ 1) for i in range(count)]
    odd = lax.ppermute(outgoing, "seq", swap)
    return convolve(rows, [back_two, (odd, 1), back_one, (odd, 0), signal],
                    gate, skip, group_width)


def solution(mesh):
    placed = (P(("rep", "seq"), None), P(("rep", "seq"), None), P(), P("seq", None))
    return jax.shard_map(
        body, mesh=mesh, in_specs=placed, out_specs=P(("rep", "seq"), None), check_vma=False
    )
```
